768 devices in a mesh: section: 6 (over z_hi, core), seq: 16 (over x, z_lo), head: 8 (over y).
Axes of the slice: x: 4, y: 8, z: 12 (z_hi: 3, z_lo: 4; z = z_hi * 4 + z_lo), core: 2. Of those that a mesh axis runs over, the one named last changes fastest.
Arguments:
- hidden: bfloat16 [6, 4096, 4096], P('section', 'seq', 'head'), may hold values from -6 to 6
- gain: bfloat16 [6, 4096], P('section'), may hold values from 0.5 to 1.5
- w_query: bfloat16 [6, 4096, 2048], P('section', None, 'head'), may hold values from -0.0234375 to 0.0234375
- w_key: bfloat16 [6, 4096, 2048], P('section', None, 'head'), may hold values from -0.09375 to 0.09375
- w_value: bfloat16 [6, 4096, 2048], P('section', None, 'head'), may hold values from -0.09375 to 0.09375
- w_out: bfloat16 [6, 2048, 4096], P('section', 'head'), may hold values from -0.5 to 0.5
- memory: bfloat16 [3072, 4096], P(('section', 'seq', 'head')), may hold values from -6 to 6
- keep: int32 [3072], P(('section', 'seq', 'head')), may hold values 0 or 1
Outputs:
- next_inputs: bfloat16 [6, 4096, 4096], P('section', 'seq', 'head')
The draws below stay inside these ranges and needn't reach their ends.
All inputs are finite; a program needn't handle non-finite values. No bound on the sum of `keep` on one device may be relied on, other than what follows from the above.
Results may differ from the reference program's by a relative error of at most 0.014.
Values may be sent and summed in bfloat16 or wider, within the bound.
No kernel may reach another device: no remote copies, remote signals or barrier semaphores. Data moves between devices by JAX's collectives and lax.ppermute only.
A program may use at most 64 MiB of HBM per device.

```python
import jax
import jax.numpy as jnp
from jax import lax

D = 4096
HEADS = 32
HEAD_DIM = 64
SECTIONS = 6
QTOK = 4096
MTOK = 3072


def set_ends(drawn, stream_key, low, largest):
    dims = drawn.shape
    spot = [jax.random.randint(jax.random.fold_in(stream_key, axis), (), 0, dims[axis]) for axis in range(len(dims))]
    drawn = drawn.at[tuple(spot)].set(low)
    longest = dims.index(max(dims))
    spot[longest] = (spot[longest] + 1) % dims[longest]
    return drawn.at[tuple(spot)].set(largest)


def level_of(own_key, shape, pieces, low, largest):
    loudness, own = 1.0, jax.random.fold_in(own_key, 6)
    for position, parts in pieces:
        steps = jnp.exp(jax.random.uniform(jax.random.fold_in(own, position), (parts,), jnp.float32, low / len(pieces), largest / len(pieces)))
        loudness = loudness * jnp.repeat(steps, shape[position] // parts).reshape([-1 if axis == position else 1 for axis in range(len(shape))])
    return loudness


def scatter_about(own_key, extent, scale, reach, pieces=(), held_as=jnp.bfloat16):
    drawn = jax.random.normal(own_key, extent, jnp.float32) * scale
    if len(pieces) > 0:
        drawn = level_of(own_key, extent, pieces, -0.22, 0.18) * drawn
    return jnp.clip(drawn, min=-reach, max=reach).astype(held_as)


def setup_inputs(seed: int = 0) -> dict:
    keys = jax.random.split(jax.random.key(seed), 9)
    hidden = scatter_about(keys[0], (SECTIONS, QTOK, D), 1.0, 6.0, ((0, 6), (1, 16), (2, 8)))
    gain = jnp.clip(1.0 + 0.1 * jax.random.normal(keys[1], (SECTIONS, D), jnp.float32), 0.5, 1.5).astype(jnp.bfloat16)
    w_query = scatter_about(keys[2], (SECTIONS, D, HEADS * HEAD_DIM), (16 * D) ** -0.5, 0.0234375, ((0, 6), (2, 8)))
    w_key = scatter_about(keys[3], (SECTIONS, D, HEADS * HEAD_DIM), D ** -0.5, 0.09375, ((0, 6), (2, 8)))
    w_value = scatter_about(keys[4], (SECTIONS, D, HEADS * HEAD_DIM), D ** -0.5, 0.09375, ((0, 6), (2, 8)))
    w_out = scatter_about(keys[5], (SECTIONS, HEADS * HEAD_DIM, D), 128 ** -0.5, 0.5, ((0, 6), (1, 8)))
    memory = scatter_about(keys[6], (MTOK, D), 1.0, 6.0, ((0, 768),))
    keep = set_ends((jax.random.randint(keys[7], (MTOK,), 0, 8) < 7).astype(jnp.int32), jax.random.fold_in(keys[7], 1), 0, 1)
    return dict(hidden=hidden, gain=gain, w_query=w_query, w_key=w_key, w_value=w_value, w_out=w_out, memory=memory, keep=keep)


def section_update(items, memory, mask_bias):
    features, gain_row, query_weight, key_weight, value_weight, out_weight = items
    widened = features.astype(jnp.float32)
    inverse = lax.rsqrt(lax.optimization_barrier(jnp.mean(widened * widened, axis=1, keepdims=True)) + 1e-06)
    normed = (widened * inverse * gain_row.astype(jnp.float32)[None, :]).astype(jnp.bfloat16)
    query = jnp.dot(normed, query_weight, preferred_element_type=jnp.float32).astype(jnp.bfloat16)
    key_rows = jnp.dot(memory, key_weight, preferred_element_type=jnp.float32).astype(jnp.bfloat16)
    value_rows = jnp.dot(memory, value_weight, preferred_element_type=jnp.float32).astype(jnp.bfloat16)
    query_heads = query.reshape(QTOK, HEADS, HEAD_DIM).transpose(1, 0, 2)
    key_heads = key_rows.reshape(MTOK, HEADS, HEAD_DIM).transpose(1, 0, 2)
    value_heads = value_rows.reshape(MTOK, HEADS, HEAD_DIM).transpose(1, 0, 2)

    def one_head(triple):
        query_head, key_head, value_head = triple
        scores = jnp.dot(query_head, key_head.T, preferred_element_type=jnp.float32) + mask_bias[None, :]
        weights = jnp.exp(scores)
        denominator = lax.optimization_barrier(jnp.sum(weights, axis=1, keepdims=True))
        numerator = jnp.dot(weights.astype(jnp.bfloat16), value_head, preferred_element_type=jnp.float32)
        return (numerator / denominator).astype(jnp.bfloat16)
    attended = lax.map(one_head, (query_heads, key_heads, value_heads))
    attended = attended.transpose(1, 0, 2).reshape(QTOK, HEADS * HEAD_DIM)
    return jnp.dot(attended, out_weight, preferred_element_type=jnp.float32).astype(jnp.bfloat16)

def reference(hidden, gain, w_query, w_key, w_value, w_out, memory, keep):
    mask_bias = (keep.astype(jnp.float32) - 1.0) * 30.0

    def per_section(items):
        return section_update(items, memory, mask_bias)
    updates = lax.map(per_section, (hidden, gain, w_query, w_key, w_value, w_out))
    return jnp.roll(updates, 1, axis=0)
```

```python
import jax
import jax.numpy as jnp
from jax import lax
from jax.sharding import Mesh, PartitionSpec as P

HEAD_DIM = 64
FLAG_PAD = 128

mask_drop = 30.0
norm_eps = 1e-06

SECTION = ("zh", "core")
SEQ = ("x", "zl")
HEAD = "y"


def shifted(x, axis, by):
    length = lax.axis_size(axis)
    return lax.ppermute(x, axis, [(i, (i + by) % length) for i in range(length)])


def ring_gather(x, axis):
    length = lax.axis_size(axis)
    pieces = {0: x}
    left, right = x, x
    for step in range(1, length // 2 + 1):
        left = shifted(left, axis, 1)
        pieces[-step % length] = left
        if step < length - step:
            right = shifted(right, axis, -1)
            pieces[step] = right
    ordered = jnp.stack([pieces[r] for r in range(length)])
    return jnp.roll(ordered, lax.axis_index(axis), axis=0)


def attend_terms(query, key_rows, value_rows, key_flags):
    head_count = query.shape[1] // HEAD_DIM
    query_heads = query.reshape(query.shape[0], head_count, HEAD_DIM)
    key_heads = key_rows.reshape(key_rows.shape[0], head_count, HEAD_DIM)
    value_heads = value_rows.reshape(value_rows.shape[0], head_count, HEAD_DIM)
    scores = jnp.einsum("qhd,khd->hqk", query_heads, key_heads, preferred_element_type=jnp.float32)
    scores = scores + ((key_flags.astype(jnp.float32) - 1.0) * mask_drop)[None, None, :]
    weights = jnp.exp(scores)
    numerator = jnp.einsum(
        "hqk,khd->qhd",
        weights.astype(jnp.bfloat16),
        value_heads,
        preferred_element_type=jnp.float32,
    )
    denominator = jnp.sum(weights, axis=2).T
    return (numerator.reshape(query.shape[0], head_count * HEAD_DIM), denominator)


def shards(hidden, gain, w_query, w_key, w_value, w_out, memory, keep):
    model = memory.shape[1]
    flags = jnp.zeros((memory.shape[0], FLAG_PAD), jnp.bfloat16)
    flags = flags.at[:, 0].set(keep.astype(jnp.bfloat16))
    packed = jnp.concatenate([memory, flags], axis=1)
    packed = lax.all_gather(packed, "core", axis=0, tiled=True)
    packed = lax.all_gather(packed, "zh", axis=0, tiled=True)
    packed = lax.all_gather(packed, HEAD, axis=0, tiled=True)
    encoder_rows = packed[:, :model]
    key_rows = jnp.dot(encoder_rows, w_key[0], preferred_element_type=jnp.float32).astype(jnp.bfloat16)
    value_rows = jnp.dot(encoder_rows, w_value[0], preferred_element_type=jnp.float32).astype(
        jnp.bfloat16
    )
    width = key_rows.shape[1]
    kv = jnp.concatenate([key_rows, value_rows, packed[:, model:]], axis=1)
    kv = lax.all_gather(kv, "zl", axis=0, tiled=True)
    kv = lax.all_gather(kv, "x", axis=0, tiled=True)

    local = hidden[0]
    gathered = ring_gather(local, HEAD)
    features = jnp.transpose(gathered, (1, 0, 2)).reshape(local.shape[0], -1)
    widened = features.astype(jnp.float32)
    inverse = lax.rsqrt(jnp.mean(widened * widened, axis=1, keepdims=True) + norm_eps)
    normed = (widened * inverse * gain[0].astype(jnp.float32)[None, :]).astype(jnp.bfloat16)
    query = jnp.dot(normed, w_query[0], preferred_element_type=jnp.float32).astype(jnp.bfloat16)

    more_num, more_den = attend_terms(
        query, kv[:, :width], kv[:, width : 2 * width], kv[:, 2 * width]
    )
    spread = jnp.repeat(more_den, HEAD_DIM, axis=1)
    attended = (more_num / spread).astype(jnp.bfloat16)
    partial_terms = jnp.dot(attended, w_out[0], preferred_element_type=jnp.float32)
    update = lax.psum_scatter(
        partial_terms.astype(jnp.bfloat16), HEAD, scatter_dimension=1, tiled=True
    )
    moved = shifted(update, SECTION, 1)
    return moved[None]


def solution(mesh):
    sizes = dict(mesh.shape)
    devices = mesh.devices.reshape(
        sizes["section"] // 2, 2, 4, sizes["seq"] // 4, sizes["head"]
    )
    fine = Mesh(devices, ("zh", "core", "x", "zl", "y"))
    everything = SECTION + SEQ + (HEAD,)
    in_specs = (
        P(SECTION, SEQ, HEAD),
        P(SECTION, None),
        P(SECTION, None, HEAD),
        P(SECTION, None, HEAD),
        P(SECTION, None, HEAD),
        P(SECTION, HEAD, None),
        P(everything, None),
        P(everything),
    )
    out_specs = P(SECTION, SEQ, HEAD)
    return jax.shard_map(shards, mesh=fine, in_specs=in_specs, out_specs=out_specs, check_vma=False)
```

```python
import jax
import jax.numpy as jnp
from jax import lax
from jax.sharding import Mesh, PartitionSpec as P

HEAD_DIM = 64
FLAG_PAD = 128

mask_drop = 30.0
norm_eps = 1e-06

SECTION = ("zh", "core")
SEQ = ("x", "zl")
HEAD = "y"


def shifted(x, axis, by):
    length = lax.axis_size(axis)
    return lax.ppermute(x, axis, [(i, (i + by) % length) for i in range(length)])


def ring_gather(x, axis):
    length = lax.axis_size(axis)
    pieces = {0: x}
    left, right = x, x
    for step in range(1, length // 2 + 1):
        left = shifted(left, axis, 1)
        pieces[-step % length] = left
        if step < length - step:
            right = shifted(right, axis, -1)
            pieces[step] = right
    ordered = jnp.stack([pieces[r] for r in range(length)])
    return jnp.roll(ordered, lax.axis_index(axis), axis=0)


def attend_terms(query, key_rows, value_rows, key_flags):
    head_count = query.shape[1] // HEAD_DIM
    query_heads = query.reshape(query.shape[0], head_count, HEAD_DIM)
    key_heads = key_rows.reshape(key_rows.shape[0], head_count, HEAD_DIM)
    value_heads = value_rows.reshape(value_rows.shape[0], head_count, HEAD_DIM)
    scores = jnp.einsum("qhd,khd->hqk", query_heads, key_heads, preferred_element_type=jnp.float32)
    scores = scores + ((key_flags.astype(jnp.float32) - 1.0) * mask_drop)[None, None, :]
    weights = jnp.exp(scores)
    numerator = jnp.einsum(
        "hqk,khd->qhd",
        weights.astype(jnp.bfloat16),
        value_heads,
        preferred_element_type=jnp.float32,
    )
    denominator = jnp.sum(weights, axis=2).T
    return (numerator.reshape(query.shape[0], head_count * HEAD_DIM), denominator)


def gather_rows(packed):
    packed = lax.all_gather(packed, "core", axis=0, tiled=True)
    packed = lax.all_gather(packed, "zh", axis=0, tiled=True)
    return lax.all_gather(packed, HEAD, axis=0, tiled=True)


def key_value_rows(packed, w_key, w_value, model):
    encoder_rows = packed[:, :model]
    key_rows = jnp.dot(encoder_rows, w_key, preferred_element_type=jnp.float32).astype(jnp.bfloat16)
    value_rows = jnp.dot(encoder_rows, w_value, preferred_element_type=jnp.float32).astype(
        jnp.bfloat16
    )
    kv = jnp.concatenate([key_rows, value_rows, packed[:, model:]], axis=1)
    kv = lax.all_gather(kv, "zl", axis=0, tiled=True)
    return lax.all_gather(kv, "x", axis=0, tiled=True)


def shards(hidden, gain, w_query, w_key, w_value, w_out, memory, keep):
    model = memory.shape[1]
    width = w_key.shape[2]
    flags = jnp.zeros((memory.shape[0], FLAG_PAD), jnp.bfloat16)
    flags = flags.at[:, 0].set(keep.astype(jnp.bfloat16))
    packed = jnp.concatenate([memory, flags], axis=1)
    halves = packed.shape[0] // 2
    kv_parts = [
        key_value_rows(gather_rows(packed[i * halves : (i + 1) * halves]), w_key[0], w_value[0], model)
        for i in range(2)
    ]

    local = hidden[0]
    gathered = ring_gather(local, HEAD)
    features = jnp.transpose(gathered, (1, 0, 2)).reshape(local.shape[0], -1)
    widened = features.astype(jnp.float32)
    inverse = lax.rsqrt(jnp.mean(widened * widened, axis=1, keepdims=True) + norm_eps)
    normed = (widened * inverse * gain[0].astype(jnp.float32)[None, :]).astype(jnp.bfloat16)
    query = jnp.dot(normed, w_query[0], preferred_element_type=jnp.float32).astype(jnp.bfloat16)

    more_num, more_den = None, None
    for kv in kv_parts:
        part_num, part_den = attend_terms(
            query, kv[:, :width], kv[:, width : 2 * width], kv[:, 2 * width]
        )
        if more_num is None:
            more_num, more_den = part_num, part_den
        else:
            more_num, more_den = more_num + part_num, more_den + part_den
    spread = jnp.repeat(more_den, HEAD_DIM, axis=1)
    attended = (more_num / spread).astype(jnp.bfloat16)
    tokens = attended.shape[0] // 2
    moved = []
    for i in range(2):
        partial_terms = jnp.dot(
            attended[i * tokens : (i + 1) * tokens], w_out[0], preferred_element_type=jnp.float32
        )
        update = lax.psum_scatter(
            partial_terms.astype(jnp.bfloat16), HEAD, scatter_dimension=1, tiled=True
        )
        moved.append(shifted(update, SECTION, 1))
    return jnp.concatenate(moved, axis=0)[None]


def solution(mesh):
    sizes = dict(mesh.shape)
    devices = mesh.devices.reshape(
        sizes["section"] // 2, 2, 4, sizes["seq"] // 4, sizes["head"]
    )
    fine = Mesh(devices, ("zh", "core", "x", "zl", "y"))
    everything = SECTION + SEQ + (HEAD,)
    in_specs = (
        P(SECTION, SEQ, HEAD),
        P(SECTION, None),
        P(SECTION, None, HEAD),
        P(SECTION, None, HEAD),
        P(SECTION, None, HEAD),
        P(SECTION, HEAD, None),
        P(everything, None),
        P(everything),
    )
    out_specs = P(SECTION, SEQ, HEAD)
    return jax.shard_map(shards, mesh=fine, in_specs=in_specs, out_specs=out_specs, check_vma=False)
```

```python
import jax
import jax.numpy as jnp
from jax import lax
from jax.sharding import Mesh, PartitionSpec as P

HEAD_DIM = 64
FLAG_PAD = 128

mask_drop = 30.0
norm_eps = 1e-06

SECTION = ("zh", "core")
SEQ = ("x", "zl")
HEAD = "y"


def shifted(x, axis, by):
    length = lax.axis_size(axis)
    return lax.ppermute(x, axis, [(i, (i + by) % length) for i in range(length)])


def ring_gather(x, axis):
    length = lax.axis_size(axis)
    pieces = {0: x}
    left, right = x, x
    for step in range(1, length // 2 + 1):
        left = shifted(left, axis, 1)
        pieces[-step % length] = left
        if step < length - step:
            right = shifted(right, axis, -1)
            pieces[step] = right
    ordered = jnp.stack([pieces[r] for r in range(length)])
    return jnp.roll(ordered, lax.axis_index(axis), axis=0)


def attend_terms(query, key_rows, value_rows, key_flags):
    head_count = query.shape[1] // HEAD_DIM
    query_heads = query.reshape(query.shape[0], head_count, HEAD_DIM)
    key_heads = key_rows.reshape(key_rows.shape[0], head_count, HEAD_DIM)
    value_heads = value_rows.reshape(value_rows.shape[0], head_count, HEAD_DIM)
    scores = jnp.einsum("qhd,khd->hqk", query_heads, key_heads, preferred_element_type=jnp.float32)
    scores = scores + ((key_flags.astype(jnp.float32) - 1.0) * mask_drop)[None, None, :]
    weights = jnp.exp(scores)
    numerator = jnp.einsum(
        "hqk,khd->qhd",
        weights.astype(jnp.bfloat16),
        value_heads,
        preferred_element_type=jnp.float32,
    )
    denominator = jnp.sum(weights, axis=2).T
    return (numerator.reshape(query.shape[0], head_count * HEAD_DIM), denominator)


def shards(hidden, gain, w_query, w_key, w_value, w_out, memory, keep):
    model = memory.shape[1]
    flags = jnp.zeros((memory.shape[0], FLAG_PAD), jnp.bfloat16)
    flags = flags.at[:, 0].set(keep.astype(jnp.bfloat16))
    packed = jnp.concatenate([memory, flags], axis=1)
    packed = lax.all_gather(packed, "core", axis=0, tiled=True)
    packed = lax.all_gather(packed, "zh", axis=0, tiled=True)
    packed = lax.all_gather(packed, HEAD, axis=0, tiled=True)
    encoder_rows = packed[:, :model]
    key_rows = jnp.dot(encoder_rows, w_key[0], preferred_element_type=jnp.float32).astype(jnp.bfloat16)
    value_rows = jnp.dot(encoder_rows, w_value[0], preferred_element_type=jnp.float32).astype(
        jnp.bfloat16
    )
    width = key_rows.shape[1]
    kv = jnp.concatenate([key_rows, value_rows, packed[:, model:]], axis=1)
    kv = lax.all_gather(kv, "zl", axis=0, tiled=True)
    kv = lax.all_gather(kv, "x", axis=0, tiled=True)

    local = hidden[0]
    gathered = ring_gather(local, HEAD)
    features = jnp.transpose(gathered, (1, 0, 2)).reshape(local.shape[0], -1)
    widened = features.astype(jnp.float32)
    inverse = lax.rsqrt(jnp.mean(widened * widened, axis=1, keepdims=True) + norm_eps)
    normed = (widened * inverse * gain[0].astype(jnp.float32)[None, :]).astype(jnp.bfloat16)
    query = jnp.dot(normed, w_query[0], preferred_element_type=jnp.float32).astype(jnp.bfloat16)

    more_num, more_den = attend_terms(
        query, kv[:, :width], kv[:, width : 2 * width], kv[:, 2 * width]
    )
    spread = jnp.repeat(more_den, HEAD_DIM, axis=1)
    attended = (more_num / spread).astype(jnp.bfloat16)
    out_cols = w_out.shape[2] // lax.axis_size(HEAD)
    out_block = lax.all_to_all(
        w_out[0].reshape(w_out.shape[1], lax.axis_size(HEAD), out_cols), HEAD, 1, 0, tiled=True
    ).reshape(-1, out_cols)
    every_head = lax.all_gather(attended, HEAD, axis=1, tiled=True)
    update = jnp.dot(every_head, out_block, preferred_element_type=jnp.float32).astype(jnp.bfloat16)
    moved = shifted(update, SECTION, 1)
    return moved[None]


def solution(mesh):
    sizes = dict(mesh.shape)
    devices = mesh.devices.reshape(
        sizes["section"] // 2, 2, 4, sizes["seq"] // 4, sizes["head"]
    )
    fine = Mesh(devices, ("zh", "core", "x", "zl", "y"))
    everything = SECTION + SEQ + (HEAD,)
    in_specs = (
        P(SECTION, SEQ, HEAD),
        P(SECTION, None),
        P(SECTION, None, HEAD),
        P(SECTION, None, HEAD),
        P(SECTION, None, HEAD),
        P(SECTION, HEAD, None),
        P(everything, None),
        P(everything),
    )
    out_specs = P(SECTION, SEQ, HEAD)
    return jax.shard_map(shards, mesh=fine, in_specs=in_specs, out_specs=out_specs, check_vma=False)
```

```python
import jax
import jax.numpy as jnp
from jax import lax
from jax.sharding import Mesh, PartitionSpec as P

HEAD_DIM = 64
FLAG_PAD = 128

mask_drop = 30.0
norm_eps = 1e-06

SECTION = ("zh", "core")
SEQ = ("x", "zl")
HEAD = "y"


def shifted(x, axis, by):
    length = lax.axis_size(axis)
    return lax.ppermute(x, axis, [(i, (i + by) % length) for i in range(length)])


def ring_gather(x, axis):
    length = lax.axis_size(axis)
    pieces = {0: x}
    left, right = x, x
    for step in range(1, length // 2 + 1):
        left = shifted(left, axis, 1)
        pieces[-step % length] = left
        if step < length - step:
            right = shifted(right, axis, -1)
            pieces[step] = right
    return jnp.concatenate([pieces[r] for r in range(length)], axis=0)


def attend_terms(query, key_rows, value_rows, key_flags):
    head_count = query.shape[1] // HEAD_DIM
    query_heads = query.reshape(query.shape[0], head_count, HEAD_DIM)
    key_heads = key_rows.reshape(key_rows.shape[0], head_count, HEAD_DIM)
    value_heads = value_rows.reshape(value_rows.shape[0], head_count, HEAD_DIM)
    scores = jnp.einsum("qhd,khd->hqk", query_heads, key_heads, preferred_element_type=jnp.float32)
    scores = scores + ((key_flags.astype(jnp.float32) - 1.0) * mask_drop)[None, None, :]
    weights = jnp.exp(scores)
    numerator = jnp.einsum(
        "hqk,khd->qhd",
        weights.astype(jnp.bfloat16),
        value_heads,
        preferred_element_type=jnp.float32,
    )
    denominator = jnp.sum(weights, axis=2).T
    return (numerator.reshape(query.shape[0], head_count * HEAD_DIM), denominator)


def shards(hidden, gain, w_query, w_key, w_value, w_out, memory, keep):
    model = memory.shape[1]
    flags = jnp.zeros((memory.shape[0], FLAG_PAD), jnp.bfloat16)
    flags = flags.at[:, 0].set(keep.astype(jnp.bfloat16))
    packed = jnp.concatenate([memory, flags], axis=1)
    packed = lax.all_gather(packed, "core", axis=0, tiled=True)
    packed = ring_gather(packed, "zh")
    packed = lax.all_gather(packed, HEAD, axis=0, tiled=True)
    encoder_rows = packed[:, :model]
    key_rows = jnp.dot(encoder_rows, w_key[0], preferred_element_type=jnp.float32).astype(jnp.bfloat16)
    value_rows = jnp.dot(encoder_rows, w_value[0], preferred_element_type=jnp.float32).astype(
        jnp.bfloat16
    )
    width = key_rows.shape[1]
    kv = jnp.concatenate([key_rows, value_rows, packed[:, model:]], axis=1)
    kv = lax.all_gather(kv, "zl", axis=0, tiled=True)
    kv = ring_gather(kv, "x")

    local = hidden[0]
    features = lax.all_gather(local, HEAD, axis=1, tiled=True)
    widened = features.astype(jnp.float32)
    inverse = lax.rsqrt(jnp.mean(widened * widened, axis=1, keepdims=True) + norm_eps)
    normed = (widened * inverse * gain[0].astype(jnp.float32)[None, :]).astype(jnp.bfloat16)
    query = jnp.dot(normed, w_query[0], preferred_element_type=jnp.float32).astype(jnp.bfloat16)

    more_num, more_den = attend_terms(
        query, kv[:, :width], kv[:, width : 2 * width], kv[:, 2 * width]
    )
    spread = jnp.repeat(more_den, HEAD_DIM, axis=1)
    attended = (more_num / spread).astype(jnp.bfloat16)
    partial_terms = jnp.dot(attended, w_out[0], preferred_element_type=jnp.float32)
    update = lax.psum_scatter(
        partial_terms.astype(jnp.bfloat16), HEAD, scatter_dimension=1, tiled=True
    )
    moved = shifted(update, SECTION, 1)
    return moved[None]


def solution(mesh):
    sizes = dict(mesh.shape)
    devices = mesh.devices.reshape(
        sizes["section"] // 2, 2, 4, sizes["seq"] // 4, sizes["head"]
    )
    fine = Mesh(devices, ("zh", "core", "x", "zl", "y"))
    everything = SECTION + SEQ + (HEAD,)
    in_specs = (
        P(SECTION, SEQ, HEAD),
        P(SECTION, None),
        P(SECTION, None, HEAD),
        P(SECTION, None, HEAD),
        P(SECTION, None, HEAD),
        P(SECTION, HEAD, None),
        P(everything, None),
        P(everything),
    )
    out_specs = P(SECTION, SEQ, HEAD)
    return jax.shard_map(shards, mesh=fine, in_specs=in_specs, out_specs=out_specs, check_vma=False)
```

```python
import jax
import jax.numpy as jnp
from jax import lax
from jax.sharding import Mesh, PartitionSpec as P

HEAD_DIM = 64
FLAG_PAD = 128

mask_drop = 30.0
norm_eps = 1e-06

SECTION = ("zh", "core")
SEQ = ("x", "zl")
HEAD = "y"


def shifted(x, axis, by):
    length = lax.axis_size(axis)
    return lax.ppermute(x, axis, [(i, (i + by) % length) for i in range(length)])


def ring_gather(x, axis):
    length = lax.axis_size(axis)
    pieces = {0: x}
    left, right = x, x
    for step in range(1, length // 2 + 1):
        if step == length - step:
            half = x.shape[0] // 2
            pieces[step] = jnp.concatenate(
                [shifted(left[:half], axis, 1), shifted(right[half:], axis, -1)], axis=0
            )
            break
        left = shifted(left, axis, 1)
        pieces[-step % length] = left
        if step < length - step:
            right = shifted(right, axis, -1)
            pieces[step] = right
    return jnp.concatenate([pieces[r] for r in range(length)], axis=0)


def attend_terms(query, key_rows, value_rows, key_flags):
    head_count = query.shape[1] // HEAD_DIM
    query_heads = query.reshape(query.shape[0], head_count, HEAD_DIM)
    key_heads = key_rows.reshape(key_rows.shape[0], head_count, HEAD_DIM)
    value_heads = value_rows.reshape(value_rows.shape[0], head_count, HEAD_DIM)
    scores = jnp.einsum("qhd,khd->hqk", query_heads, key_heads, preferred_element_type=jnp.float32)
    scores = scores + ((key_flags.astype(jnp.float32) - 1.0) * mask_drop)[None, None, :]
    weights = jnp.exp(scores)
    numerator = jnp.einsum(
        "hqk,khd->qhd",
        weights.astype(jnp.bfloat16),
        value_heads,
        preferred_element_type=jnp.float32,
    )
    denominator = jnp.sum(weights, axis=2).T
    return (numerator.reshape(query.shape[0], head_count * HEAD_DIM), denominator)


def shards(hidden, gain, w_query, w_key, w_value, w_out, memory, keep):
    model = memory.shape[1]
    flags = jnp.zeros((memory.shape[0], FLAG_PAD), jnp.bfloat16)
    flags = flags.at[:, 0].set(keep.astype(jnp.bfloat16))
    packed = jnp.concatenate([memory, flags], axis=1)
    packed = lax.all_gather(packed, "core", axis=0, tiled=True)
    packed = lax.all_gather(packed, "zh", axis=0, tiled=True)
    packed = lax.all_gather(packed, HEAD, axis=0, tiled=True)
    encoder_rows = packed[:, :model]
    key_rows = jnp.dot(encoder_rows, w_key[0], preferred_element_type=jnp.float32).astype(jnp.bfloat16)
    value_rows = jnp.dot(encoder_rows, w_value[0], preferred_element_type=jnp.float32).astype(
        jnp.bfloat16
    )
    width = key_rows.shape[1]
    rows = key_rows.shape[0]
    flag_rows = jnp.zeros((8, 2 * width), jnp.bfloat16)
    flag_rows = flag_rows.at[0, :rows].set(packed[:, model])
    kv = jnp.concatenate([key_rows, value_rows], axis=1)
    kv = jnp.concatenate([kv, flag_rows], axis=0)
    kv = lax.all_gather(kv, "zl", axis=0, tiled=True)
    kv = ring_gather(kv, "x")
    kv = kv.reshape(-1, rows + 8, 2 * width)
    key_flags = kv[:, rows, :rows].reshape(-1)
    kv = kv[:, :rows].reshape(-1, 2 * width)

    local = hidden[0]
    features = lax.all_gather(local, HEAD, axis=1, tiled=True)
    widened = features.astype(jnp.float32)
    inverse = lax.rsqrt(jnp.mean(widened * widened, axis=1, keepdims=True) + norm_eps)
    normed = (widened * inverse * gain[0].astype(jnp.float32)[None, :]).astype(jnp.bfloat16)
    query = jnp.dot(normed, w_query[0], preferred_element_type=jnp.float32).astype(jnp.bfloat16)

    more_num, more_den = attend_terms(
        query, kv[:, :width], kv[:, width:], key_flags
    )
    spread = jnp.repeat(more_den, HEAD_DIM, axis=1)
    attended = (more_num / spread).astype(jnp.bfloat16)
    partial_terms = jnp.dot(attended, w_out[0], preferred_element_type=jnp.float32)
    update = lax.psum_scatter(
        partial_terms.astype(jnp.bfloat16), HEAD, scatter_dimension=1, tiled=True
    )
    moved = shifted(update, SECTION, 1)
    return moved[None]


def solution(mesh):
    sizes = dict(mesh.shape)
    devices = mesh.devices.reshape(
        sizes["section"] // 2, 2, 4, sizes["seq"] // 4, sizes["head"]
    )
    fine = Mesh(devices, ("zh", "core", "x", "zl", "y"))
    everything = SECTION + SEQ + (HEAD,)
    in_specs = (
        P(SECTION, SEQ, HEAD),
        P(SECTION, None),
        P(SECTION, None, HEAD),
        P(SECTION, None, HEAD),
        P(SECTION, None, HEAD),
        P(SECTION, HEAD, None),
        P(everything, None),
        P(everything),
    )
    out_specs = P(SECTION, SEQ, HEAD)
    return jax.shard_map(shards, mesh=fine, in_specs=in_specs, out_specs=out_specs, check_vma=False)
```

```python
import jax
import jax.numpy as jnp
from jax import lax
from jax.sharding import Mesh, PartitionSpec as P

HEAD_DIM = 64
FLAG_PAD = 128

mask_drop = 30.0
norm_eps = 1e-06

SECTION = ("zh", "core")
SEQ = ("x", "zl")
HEAD = "y"


def shifted(x, axis, by):
    length = lax.axis_size(axis)
    return lax.ppermute(x, axis, [(i, (i + by) % length) for i in range(length)])


def ring_gather(x, axis):
    length = lax.axis_size(axis)
    pieces = {0: x}
    left, right = x, x
    for step in range(1, length // 2 + 1):
        if step == length - step:
            half = x.shape[0] // 2
            pieces[step] = jnp.concatenate(
                [shifted(left[:half], axis, 1), shifted(right[half:], axis, -1)], axis=0
            )
            break
        left = shifted(left, axis, 1)
        pieces[-step % length] = left
        if step < length - step:
            right = shifted(right, axis, -1)
            pieces[step] = right
    return jnp.concatenate([pieces[r] for r in range(length)], axis=0)


def attend_terms(query, key_rows, value_rows, key_flags, real_rows):
    head_count = query.shape[1] // HEAD_DIM
    query_heads = query.reshape(query.shape[0], head_count, HEAD_DIM)
    key_heads = key_rows.reshape(key_rows.shape[0], head_count, HEAD_DIM)
    value_heads = value_rows.reshape(value_rows.shape[0], head_count, HEAD_DIM)
    scores = jnp.einsum("qhd,khd->hqk", query_heads, key_heads, preferred_element_type=jnp.float32)
    scores = scores + ((key_flags.astype(jnp.float32) - 1.0) * mask_drop)[None, None, :]
    weights = jnp.where(real_rows[None, None, :], jnp.exp(scores), 0.0)
    numerator = jnp.einsum(
        "hqk,khd->qhd",
        weights.astype(jnp.bfloat16),
        value_heads,
        preferred_element_type=jnp.float32,
    )
    denominator = jnp.sum(weights, axis=2).T
    return (numerator.reshape(query.shape[0], head_count * HEAD_DIM), denominator)


def shards(hidden, gain, w_query, w_key, w_value, w_out, memory, keep):
    model = memory.shape[1]
    flags = jnp.zeros((memory.shape[0], FLAG_PAD), jnp.bfloat16)
    flags = flags.at[:, 0].set(keep.astype(jnp.bfloat16))
    packed = jnp.concatenate([memory, flags], axis=1)
    packed = lax.all_gather(packed, "core", axis=0, tiled=True)
    packed = lax.all_gather(packed, "zh", axis=0, tiled=True)
    packed = lax.all_gather(packed, HEAD, axis=0, tiled=True)
    encoder_rows = packed[:, :model]
    key_rows = jnp.dot(encoder_rows, w_key[0], preferred_element_type=jnp.float32).astype(jnp.bfloat16)
    value_rows = jnp.dot(encoder_rows, w_value[0], preferred_element_type=jnp.float32).astype(
        jnp.bfloat16
    )
    width = key_rows.shape[1]
    rows = key_rows.shape[0]
    flag_rows = jnp.zeros((8, 2 * width), jnp.bfloat16)
    flag_rows = flag_rows.at[0, :rows].set(packed[:, model])
    kv = jnp.concatenate([key_rows, value_rows], axis=1)
    kv = jnp.concatenate([kv, flag_rows], axis=0)
    kv = lax.all_gather(kv, "zl", axis=0, tiled=True)
    kv = ring_gather(kv, "x")
    blocks = kv.reshape(-1, rows + 8, 2 * width)
    key_flags = jnp.pad(blocks[:, rows, :rows], ((0, 0), (0, 8))).reshape(-1)
    real_rows = (jnp.arange(rows + 8) < rows)[None, :].repeat(blocks.shape[0], 0).reshape(-1)

    local = hidden[0]
    features = lax.all_gather(local, HEAD, axis=1, tiled=True)
    widened = features.astype(jnp.float32)
    inverse = lax.rsqrt(jnp.mean(widened * widened, axis=1, keepdims=True) + norm_eps)
    normed = (widened * inverse * gain[0].astype(jnp.float32)[None, :]).astype(jnp.bfloat16)
    query = jnp.dot(normed, w_query[0], preferred_element_type=jnp.float32).astype(jnp.bfloat16)

    more_num, more_den = attend_terms(
        query, kv[:, :width], kv[:, width:], key_flags, real_rows
    )
    spread = jnp.repeat(more_den, HEAD_DIM, axis=1)
    attended = (more_num / spread).astype(jnp.bfloat16)
    partial_terms = jnp.dot(attended, w_out[0], preferred_element_type=jnp.float32)
    update = lax.psum_scatter(
        partial_terms.astype(jnp.bfloat16), HEAD, scatter_dimension=1, tiled=True
    )
    moved = shifted(update, SECTION, 1)
    return moved[None]


def solution(mesh):
    sizes = dict(mesh.shape)
    devices = mesh.devices.reshape(
        sizes["section"] // 2, 2, 4, sizes["seq"] // 4, sizes["head"]
    )
    fine = Mesh(devices, ("zh", "core", "x", "zl", "y"))
    everything = SECTION + SEQ + (HEAD,)
    in_specs = (
        P(SECTION, SEQ, HEAD),
        P(SECTION, None),
        P(SECTION, None, HEAD),
        P(SECTION, None, HEAD),
        P(SECTION, None, HEAD),
        P(SECTION, HEAD, None),
        P(everything, None),
        P(everything),
    )
    out_specs = P(SECTION, SEQ, HEAD)
    return jax.shard_map(shards, mesh=fine, in_specs=in_specs, out_specs=out_specs, check_vma=False)
```

```python
import jax
import jax.numpy as jnp
from jax import lax
from jax.sharding import Mesh, PartitionSpec as P

HEAD_DIM = 64
FLAG_PAD = 128

mask_drop = 30.0
norm_eps = 1e-06

SECTION = ("zh", "core")
SEQ = ("x", "zl")
HEAD = "y"


def shifted(x, axis, by):
    length = lax.axis_size(axis)
    return lax.ppermute(x, axis, [(i, (i + by) % length) for i in range(length)])


def ring_gather(x, axis):
    return jnp.concatenate(ring_pieces(x, axis), axis=0)


def ring_pieces(x, axis):
    length = lax.axis_size(axis)
    pieces = {0: x}
    left, right = x, x
    for step in range(1, length // 2 + 1):
        if step == length - step:
            half = x.shape[0] // 2
            pieces[step] = jnp.concatenate(
                [shifted(left[:half], axis, 1), shifted(right[half:], axis, -1)], axis=0
            )
            break
        left = shifted(left, axis, 1)
        pieces[-step % length] = left
        if step < length - step:
            right = shifted(right, axis, -1)
            pieces[step] = right
    return [pieces[r] for r in range(length)]


def attend_terms(query, key_rows, value_rows, key_flags):
    head_count = query.shape[1] // HEAD_DIM
    query_heads = query.reshape(query.shape[0], head_count, HEAD_DIM)
    key_heads = key_rows.reshape(key_rows.shape[0], head_count, HEAD_DIM)
    value_heads = value_rows.reshape(value_rows.shape[0], head_count, HEAD_DIM)
    scores = jnp.einsum("qhd,khd->hqk", query_heads, key_heads, preferred_element_type=jnp.float32)
    scores = scores + ((key_flags.astype(jnp.float32) - 1.0) * mask_drop)[None, None, :]
    weights = jnp.exp(scores)
    numerator = jnp.einsum(
        "hqk,khd->qhd",
        weights.astype(jnp.bfloat16),
        value_heads,
        preferred_element_type=jnp.float32,
    )
    denominator = jnp.sum(weights, axis=2).T
    return (numerator.reshape(query.shape[0], head_count * HEAD_DIM), denominator)


def shards(hidden, gain, w_query, w_key, w_value, w_out, memory, keep):
    model = memory.shape[1]
    flags = jnp.zeros((memory.shape[0], FLAG_PAD), jnp.bfloat16)
    flags = flags.at[:, 0].set(keep.astype(jnp.bfloat16))
    packed = jnp.concatenate([memory, flags], axis=1)
    packed = lax.all_gather(packed, "core", axis=0, tiled=True)
    packed = lax.all_gather(packed, "zh", axis=0, tiled=True)
    both = jnp.concatenate([w_key[0], w_value[0]], axis=1)
    pieces = ring_pieces(packed, HEAD)
    kv = jnp.concatenate(
        [
            jnp.dot(p[:, :model], both, preferred_element_type=jnp.float32).astype(jnp.bfloat16)
            for p in pieces
        ],
        axis=0,
    )
    packed = jnp.concatenate([p[:, model:model + 1] for p in pieces], axis=0)
    key_rows = kv
    width = w_key.shape[2]
    rows = key_rows.shape[0]
    flag_rows = jnp.zeros((8, 2 * width), jnp.bfloat16)
    flag_rows = flag_rows.at[0, :rows].set(packed[:, 0])
    kv = jnp.concatenate([kv, flag_rows], axis=0)
    kv = lax.all_gather(kv, "zl", axis=0, tiled=True)
    kv = ring_gather(kv, "x")
    kv = kv.reshape(-1, rows + 8, 2 * width)
    key_flags = kv[:, rows, :rows].reshape(-1)
    kv = kv[:, :rows].reshape(-1, 2 * width)

    local, packed = lax.optimization_barrier((hidden[0], packed))
    features = lax.all_gather(local, HEAD, axis=1, tiled=True)
    widened = features.astype(jnp.float32)
    inverse = lax.rsqrt(jnp.mean(widened * widened, axis=1, keepdims=True) + norm_eps)
    normed = (widened * inverse * gain[0].astype(jnp.float32)[None, :]).astype(jnp.bfloat16)
    query = jnp.dot(normed, w_query[0], preferred_element_type=jnp.float32).astype(jnp.bfloat16)

    more_num, more_den = attend_terms(
        query, kv[:, :width], kv[:, width:], key_flags
    )
    spread = jnp.repeat(more_den, HEAD_DIM, axis=1)
    attended = (more_num / spread).astype(jnp.bfloat16)
    partial_terms = jnp.dot(attended, w_out[0], preferred_element_type=jnp.float32)
    update = lax.psum_scatter(
        partial_terms.astype(jnp.bfloat16), HEAD, scatter_dimension=1, tiled=True
    )
    moved = shifted(update, SECTION, 1)
    return moved[None]


def solution(mesh):
    sizes = dict(mesh.shape)
    devices = mesh.devices.reshape(
        sizes["section"] // 2, 2, 4, sizes["seq"] // 4, sizes["head"]
    )
    fine = Mesh(devices, ("zh", "core", "x", "zl", "y"))
    everything = SECTION + SEQ + (HEAD,)
    in_specs = (
        P(SECTION, SEQ, HEAD),
        P(SECTION, None),
        P(SECTION, None, HEAD),
        P(SECTION, None, HEAD),
        P(SECTION, None, HEAD),
        P(SECTION, HEAD, None),
        P(everything, None),
        P(everything),
    )
    out_specs = P(SECTION, SEQ, HEAD)
    return jax.shard_map(shards, mesh=fine, in_specs=in_specs, out_specs=out_specs, check_vma=False)
```

```python
import jax
import jax.numpy as jnp
from jax import lax
from jax.sharding import Mesh, PartitionSpec as P

HEAD_DIM = 64
FLAG_PAD = 128

mask_drop = 30.0
norm_eps = 1e-06

SECTION = ("zh", "core")
SEQ = ("x", "zl")
HEAD = "y"


def shifted(x, axis, by):
    length = lax.axis_size(axis)
    return lax.ppermute(x, axis, [(i, (i + by) % length) for i in range(length)])


def ring_gather(x, axis):
    return jnp.concatenate(ring_pieces(x, axis), axis=0)


def ring_pieces(x, axis):
    length = lax.axis_size(axis)
    pieces = {0: x}
    left, right = x, x
    for step in range(1, length // 2 + 1):
        if step == length - step:
            half = x.shape[0] // 2
            pieces[step] = jnp.concatenate(
                [shifted(left[:half], axis, 1), shifted(right[half:], axis, -1)], axis=0
            )
            break
        left = shifted(left, axis, 1)
        pieces[-step % length] = left
        if step < length - step:
            right = shifted(right, axis, -1)
            pieces[step] = right
    return [pieces[r] for r in range(length)]


def attend_terms(query, key_rows, value_rows, key_flags, real_rows):
    head_count = query.shape[1] // HEAD_DIM
    query_heads = query.reshape(query.shape[0], head_count, HEAD_DIM)
    key_heads = key_rows.reshape(key_rows.shape[0], head_count, HEAD_DIM)
    value_heads = value_rows.reshape(value_rows.shape[0], head_count, HEAD_DIM)
    scores = jnp.einsum("qhd,khd->hqk", query_heads, key_heads, preferred_element_type=jnp.float32)
    scores = scores + ((key_flags.astype(jnp.float32) - 1.0) * mask_drop)[None, None, :]
    weights = jnp.where(real_rows[None, None, :], jnp.exp(scores), 0.0)
    numerator = jnp.einsum(
        "hqk,khd->qhd",
        weights.astype(jnp.bfloat16),
        value_heads,
        preferred_element_type=jnp.float32,
    )
    denominator = jnp.sum(weights, axis=2).T
    return (numerator.reshape(query.shape[0], head_count * HEAD_DIM), denominator)


def shards(hidden, gain, w_query, w_key, w_value, w_out, memory, keep):
    model = memory.shape[1]
    flags = jnp.zeros((memory.shape[0], FLAG_PAD), jnp.bfloat16)
    flags = flags.at[:, 0].set(keep.astype(jnp.bfloat16))
    packed = jnp.concatenate([memory, flags], axis=1)
    packed = lax.all_gather(packed, "core", axis=0, tiled=True)
    packed = lax.all_gather(packed, "zh", axis=0, tiled=True)
    both = jnp.concatenate([w_key[0], w_value[0]], axis=1)
    pieces = ring_pieces(packed, HEAD)
    kv = jnp.concatenate(
        [
            jnp.dot(p[:, :model], both, preferred_element_type=jnp.float32).astype(jnp.bfloat16)
            for p in pieces
        ],
        axis=0,
    )
    packed = jnp.concatenate([p[:, model:model + 1] for p in pieces], axis=0)
    key_rows = kv
    width = w_key.shape[2]
    rows = key_rows.shape[0]
    flag_rows = jnp.zeros((8, 2 * width), jnp.bfloat16)
    flag_rows = flag_rows.at[0, :rows].set(packed[:, 0])
    kv = jnp.concatenate([kv, flag_rows], axis=0)
    kv = lax.all_gather(kv, "zl", axis=0, tiled=True)
    features = lax.all_gather(hidden[0], HEAD, axis=1, tiled=True)
    widened = features.astype(jnp.float32)
    inverse = lax.rsqrt(jnp.mean(widened * widened, axis=1, keepdims=True) + norm_eps)
    normed = (widened * inverse * gain[0].astype(jnp.float32)[None, :]).astype(jnp.bfloat16)
    query = jnp.dot(normed, w_query[0], preferred_element_type=jnp.float32).astype(jnp.bfloat16)

    kv, query = lax.optimization_barrier((kv, query))
    kv_pieces = ring_pieces(kv, "x")


    more_num, more_den = None, None
    for piece in kv_pieces:
        blocks = piece.reshape(-1, rows + 8, 2 * width)
        key_flags = jnp.pad(blocks[:, rows, :rows], ((0, 0), (0, 8))).reshape(-1)
        real_rows = (jnp.arange(rows + 8) < rows)[None, :].repeat(blocks.shape[0], 0).reshape(-1)
        part_num, part_den = attend_terms(
            query, piece[:, :width], piece[:, width:], key_flags, real_rows
        )
        if more_num is None:
            more_num, more_den = part_num, part_den
        else:
            more_num, more_den = more_num + part_num, more_den + part_den
    spread = jnp.repeat(more_den, HEAD_DIM, axis=1)
    attended = (more_num / spread).astype(jnp.bfloat16)
    partial_terms = jnp.dot(attended, w_out[0], preferred_element_type=jnp.float32)
    update = lax.psum_scatter(
        partial_terms.astype(jnp.bfloat16), HEAD, scatter_dimension=1, tiled=True
    )
    moved = shifted(update, SECTION, 1)
    return moved[None]


def solution(mesh):
    sizes = dict(mesh.shape)
    devices = mesh.devices.reshape(
        sizes["section"] // 2, 2, 4, sizes["seq"] // 4, sizes["head"]
    )
    fine = Mesh(devices, ("zh", "core", "x", "zl", "y"))
    everything = SECTION + SEQ + (HEAD,)
    in_specs = (
        P(SECTION, SEQ, HEAD),
        P(SECTION, None),
        P(SECTION, None, HEAD),
        P(SECTION, None, HEAD),
        P(SECTION, None, HEAD),
        P(SECTION, HEAD, None),
        P(everything, None),
        P(everything),
    )
    out_specs = P(SECTION, SEQ, HEAD)
    return jax.shard_map(shards, mesh=fine, in_specs=in_specs, out_specs=out_specs, check_vma=False)
```

```python
import jax
import jax.numpy as jnp
from jax import lax
from jax.sharding import Mesh, PartitionSpec as P

HEAD_DIM = 64
FLAG_PAD = 128

mask_drop = 30.0
norm_eps = 1e-06

SECTION = ("zh", "core")
SEQ = ("x", "zl")
HEAD = "y"


def shifted(x, axis, by):
    length = lax.axis_size(axis)
    return lax.ppermute(x, axis, [(i, (i + by) % length) for i in range(length)])


def ring_gather(x, axis):
    return jnp.concatenate(ring_pieces(x, axis), axis=0)


def ring_pieces(x, axis):
    length = lax.axis_size(axis)
    pieces = {0: x}
    left, right = x, x
    for step in range(1, length // 2 + 1):
        if step == length - step:
            half = x.shape[0] // 2
            pieces[step] = jnp.concatenate(
                [shifted(left[:half], axis, 1), shifted(right[half:], axis, -1)], axis=0
            )
            break
        left = shifted(left, axis, 1)
        pieces[-step % length] = left
        if step < length - step:
            right = shifted(right, axis, -1)
            pieces[step] = right
    return [pieces[r] for r in range(length)]


def attend_terms(query, key_rows, value_rows, key_flags, real_rows):
    head_count = query.shape[1] // HEAD_DIM
    query_heads = query.reshape(query.shape[0], head_count, HEAD_DIM)
    key_heads = key_rows.reshape(key_rows.shape[0], head_count, HEAD_DIM)
    value_heads = value_rows.reshape(value_rows.shape[0], head_count, HEAD_DIM)
    scores = jnp.einsum("qhd,khd->hqk", query_heads, key_heads, preferred_element_type=jnp.float32)
    scores = scores + ((key_flags.astype(jnp.float32) - 1.0) * mask_drop)[None, None, :]
    weights = jnp.where(real_rows[None, None, :], jnp.exp(scores), 0.0)
    numerator = jnp.einsum(
        "hqk,khd->qhd",
        weights.astype(jnp.bfloat16),
        value_heads,
        preferred_element_type=jnp.float32,
    )
    denominator = jnp.sum(weights, axis=2).T
    return (numerator.reshape(query.shape[0], head_count * HEAD_DIM), denominator)


def shards(hidden, gain, w_query, w_key, w_value, w_out, memory, keep):
    model = memory.shape[1]
    flags = jnp.zeros((memory.shape[0], FLAG_PAD), jnp.bfloat16)
    flags = flags.at[:, 0].set(keep.astype(jnp.bfloat16))
    packed = jnp.concatenate([memory, flags], axis=1)
    packed = lax.all_gather(packed, "core", axis=0, tiled=True)
    packed = lax.all_gather(packed, "zh", axis=0, tiled=True)
    both = jnp.concatenate([w_key[0], w_value[0]], axis=1)
    pieces = ring_pieces(packed, HEAD)
    kv = jnp.concatenate(
        [
            jnp.dot(p[:, :model], both, preferred_element_type=jnp.float32).astype(jnp.bfloat16)
            for p in pieces
        ],
        axis=0,
    )
    packed = jnp.concatenate([p[:, model:model + 1] for p in pieces], axis=0)
    key_rows = kv
    width = w_key.shape[2]
    rows = key_rows.shape[0]
    flag_rows = jnp.zeros((8, 2 * width), jnp.bfloat16)
    flag_rows = flag_rows.at[0, :rows].set(packed[:, 0])
    kv = jnp.concatenate([kv, flag_rows], axis=0)
    kv = lax.all_gather(kv, "zl", axis=0, tiled=True)
    kv_pieces = ring_pieces(kv, "x")

    local, packed = lax.optimization_barrier((hidden[0], packed))
    features = lax.all_gather(local, HEAD, axis=1, tiled=True)
    widened = features.astype(jnp.float32)
    inverse = lax.rsqrt(jnp.mean(widened * widened, axis=1, keepdims=True) + norm_eps)
    normed = (widened * inverse * gain[0].astype(jnp.float32)[None, :]).astype(jnp.bfloat16)
    query = jnp.dot(normed, w_query[0], preferred_element_type=jnp.float32).astype(jnp.bfloat16)

    more_num, more_den = None, None
    for piece in kv_pieces:
        blocks = piece.reshape(-1, rows + 8, 2 * width)
        key_flags = jnp.pad(blocks[:, rows, :rows], ((0, 0), (0, 8))).reshape(-1)
        real_rows = (jnp.arange(rows + 8) < rows)[None, :].repeat(blocks.shape[0], 0).reshape(-1)
        part_num, part_den = attend_terms(
            query, piece[:, :width], piece[:, width:], key_flags, real_rows
        )
        if more_num is None:
            more_num, more_den = part_num, part_den
        else:
            more_num, more_den = more_num + part_num, more_den + part_den
    spread = jnp.repeat(more_den, HEAD_DIM, axis=1)
    attended = (more_num / spread).astype(jnp.bfloat16)
    partial_terms = jnp.dot(attended, w_out[0], preferred_element_type=jnp.float32)
    update = lax.psum_scatter(
        partial_terms.astype(jnp.bfloat16), HEAD, scatter_dimension=1, tiled=True
    )
    moved = shifted(update, SECTION, 1)
    return moved[None]


def solution(mesh):
    sizes = dict(mesh.shape)
    devices = mesh.devices.reshape(
        sizes["section"] // 2, 2, 4, sizes["seq"] // 4, sizes["head"]
    )
    fine = Mesh(devices, ("zh", "core", "x", "zl", "y"))
    everything = SECTION + SEQ + (HEAD,)
    in_specs = (
        P(SECTION, SEQ, HEAD),
        P(SECTION, None),
        P(SECTION, None, HEAD),
        P(SECTION, None, HEAD),
        P(SECTION, None, HEAD),
        P(SECTION, HEAD, None),
        P(everything, None),
        P(everything),
    )
    out_specs = P(SECTION, SEQ, HEAD)
    return jax.shard_map(shards, mesh=fine, in_specs=in_specs, out_specs=out_specs, check_vma=False)
```

```python
import jax
import jax.numpy as jnp
from jax import lax
from jax.sharding import Mesh, PartitionSpec as P

HEAD_DIM = 64
FLAG_PAD = 128

mask_drop = 30.0
norm_eps = 1e-06

SECTION = ("zh", "core")
SEQ = ("x", "zl")
HEAD = "y"


def shifted(x, axis, by):
    length = lax.axis_size(axis)
    return lax.ppermute(x, axis, [(i, (i + by) % length) for i in range(length)])


def ring_gather(x, axis):
    return jnp.concatenate(ring_pieces(x, axis), axis=0)


def ring_pieces(x, axis):
    length = lax.axis_size(axis)
    pieces = {0: x}
    left, right = x, x
    for step in range(1, length // 2 + 1):
        if step == length - step:
            half = x.shape[0] // 2
            pieces[step] = jnp.concatenate(
                [shifted(left[:half], axis, 1), shifted(right[half:], axis, -1)], axis=0
            )
            break
        left = shifted(left, axis, 1)
        pieces[-step % length] = left
        if step < length - step:
            right = shifted(right, axis, -1)
            pieces[step] = right
    return [pieces[r] for r in range(length)]


def attend_terms(query, key_rows, value_rows, key_flags):
    head_count = query.shape[1] // HEAD_DIM
    query_heads = query.reshape(query.shape[0], head_count, HEAD_DIM)
    key_heads = key_rows.reshape(key_rows.shape[0], head_count, HEAD_DIM)
    value_heads = value_rows.reshape(value_rows.shape[0], head_count, HEAD_DIM)
    scores = jnp.einsum("qhd,khd->hqk", query_heads, key_heads, preferred_element_type=jnp.float32)
    scores = scores + ((key_flags.astype(jnp.float32) - 1.0) * mask_drop)[None, None, :]
    weights = jnp.exp(scores)
    numerator = jnp.einsum(
        "hqk,khd->qhd",
        weights.astype(jnp.bfloat16),
        value_heads,
        preferred_element_type=jnp.float32,
    )
    denominator = jnp.sum(weights, axis=2).T
    return (numerator.reshape(query.shape[0], head_count * HEAD_DIM), denominator)


def shards(hidden, gain, w_query, w_key, w_value, w_out, memory, keep):
    model = memory.shape[1]
    flags = jnp.zeros((memory.shape[0], FLAG_PAD), jnp.bfloat16)
    flags = flags.at[:, 0].set(keep.astype(jnp.bfloat16))
    packed = jnp.concatenate([memory, flags], axis=1)
    packed = lax.all_gather(packed, "core", axis=0, tiled=True)
    packed = lax.all_gather(packed, "zh", axis=0, tiled=True)
    both = jnp.concatenate([w_key[0], w_value[0]], axis=1)
    pieces = ring_pieces(packed, HEAD)
    length = len(pieces)
    groups = [[pieces[0]]] + [
        [pieces[r], pieces[-r % length]] if r != length - r else [pieces[r]]
        for r in range(1, length // 2 + 1)
    ]
    groups = [jnp.concatenate(g, axis=0) if len(g) > 1 else g[0] for g in groups]
    kv = jnp.concatenate(
        [
            jnp.dot(g[:, :model], both, preferred_element_type=jnp.float32).astype(jnp.bfloat16)
            for g in groups
        ],
        axis=0,
    )
    packed = jnp.concatenate([g[:, model:model + 1] for g in groups], axis=0)
    key_rows = kv
    width = w_key.shape[2]
    rows = key_rows.shape[0]
    flag_rows = jnp.zeros((8, 2 * width), jnp.bfloat16)
    flag_rows = flag_rows.at[0, :rows].set(packed[:, 0])
    kv = jnp.concatenate([kv, flag_rows], axis=0)
    kv = lax.all_gather(kv, "zl", axis=0, tiled=True)
    kv = ring_gather(kv, "x")
    kv = kv.reshape(-1, rows + 8, 2 * width)
    key_flags = kv[:, rows, :rows].reshape(-1)
    kv = kv[:, :rows].reshape(-1, 2 * width)

    local, packed = lax.optimization_barrier((hidden[0], packed))
    features = lax.all_gather(local, HEAD, axis=1, tiled=True)
    widened = features.astype(jnp.float32)
    inverse = lax.rsqrt(jnp.mean(widened * widened, axis=1, keepdims=True) + norm_eps)
    normed = (widened * inverse * gain[0].astype(jnp.float32)[None, :]).astype(jnp.bfloat16)
    query = jnp.dot(normed, w_query[0], preferred_element_type=jnp.float32).astype(jnp.bfloat16)

    more_num, more_den = attend_terms(
        query, kv[:, :width], kv[:, width:], key_flags
    )
    spread = jnp.repeat(more_den, HEAD_DIM, axis=1)
    attended = (more_num / spread).astype(jnp.bfloat16)
    partial_terms = jnp.dot(attended, w_out[0], preferred_element_type=jnp.float32)
    update = lax.psum_scatter(
        partial_terms.astype(jnp.bfloat16), HEAD, scatter_dimension=1, tiled=True
    )
    moved = shifted(update, SECTION, 1)
    return moved[None]


def solution(mesh):
    sizes = dict(mesh.shape)
    devices = mesh.devices.reshape(
        sizes["section"] // 2, 2, 4, sizes["seq"] // 4, sizes["head"]
    )
    fine = Mesh(devices, ("zh", "core", "x", "zl", "y"))
    everything = SECTION + SEQ + (HEAD,)
    in_specs = (
        P(SECTION, SEQ, HEAD),
        P(SECTION, None),
        P(SECTION, None, HEAD),
        P(SECTION, None, HEAD),
        P(SECTION, None, HEAD),
        P(SECTION, HEAD, None),
        P(everything, None),
        P(everything),
    )
    out_specs = P(SECTION, SEQ, HEAD)
    return jax.shard_map(shards, mesh=fine, in_specs=in_specs, out_specs=out_specs, check_vma=False)
```
